512 devices in a mesh: sep: 8 (over y), row: 8 (over z), col: 8 (over x, core).
Axes of the slice: x: 4, y: 8, z: 8, core: 2. Of those that a mesh axis runs over, the one named last changes fastest.
Arguments:
- right_sides: float32 [2, 16, 32768], P(None, None, ('sep', 'row', 'col')), may hold values from -6 to 6
- inverse_diag: float32 [8, 4096, 4096], P('sep', ('row', 'col')), may hold values from -0.09375 to 0.09375
- lower_blocks: float32 [8, 2048, 4096], P('sep', ('row', 'col')), may hold values from -0.09375 to 0.09375
- targets: int32 [8, 2048], P('sep', ('row', 'col')), may hold values from 0 to 32767, as said below
- counts: int32 [8, 64], P('sep', ('row', 'col')), may hold values from 0 to 32, as said below
Outputs:
- solution: float32 [2, 16, 32768], P(None, None, ('sep', 'row', 'col'))
The draws below stay inside these ranges and needn't reach their ends.
Inputs may be any that keep to these rules, and one draw needn't show every extreme that they name: For every separator s and lower row j: targets[s, j] // 4096 > s, except for the last separator whose counts are all zero; and (targets[s, j] % 4096) // 64 == j // 32. The last separator's counts are zero; every other separator has a block with exactly 32 live rows, and the others at least one.
All inputs are finite; a program needn't handle non-finite values.
Results may differ from the reference program's by a relative error of at most 0.0001.
Values sent between devices are 32-bit elements; how exact they have to be, the bound alone decides.
No kernel may reach another device: no remote copies, remote signals or barrier semaphores. Data moves between devices by JAX's collectives and lax.ppermute only.
A program may use at most 64 MiB of HBM per device.

```python
import jax
import jax.numpy as jnp
from jax import lax

W = 4096
LRD = 32
BRHS = 16
BATCHES = 2
SEPS = 8
SHARDS = 64
LOWER = 2048
ROWS = 32768


def draw_targets(key, part):
    first, second, third = jax.random.split(jax.random.fold_in(key, 23), 3)
    level = jnp.arange(SEPS, dtype=jnp.int32)[:, None]
    spread = jax.random.randint(first, (SEPS, LOWER), 0, 1 << 20)
    picker = jax.random.randint(third, (SEPS, LOWER), 0, 4)
    jump = jnp.where(picker == 0, spread % jnp.maximum(SEPS - 1 - level, 1), 0)
    later = jnp.minimum(level + 1 + jump, SEPS - 1)
    block = (jnp.arange(LOWER, dtype=jnp.int32) // LRD)[None, :]
    offset = jax.random.randint(second, (SEPS, LOWER), 0, W // SHARDS)
    return (later * W + block * (W // SHARDS) + offset).astype(jnp.int32)


def draw_counts(key, part):
    first, second = jax.random.split(jax.random.fold_in(key, 11))
    base = jax.random.randint(first, (SEPS, SHARDS), 1, LRD + 1)
    fullest = jax.random.randint(second, (SEPS, 1), 0, SHARDS)
    columns = jnp.arange(SHARDS, dtype=jnp.int32)[None, :]
    base = jnp.where(columns == fullest, LRD, base)
    finale = jnp.arange(SEPS, dtype=jnp.int32)[:, None] == SEPS - 1
    return jnp.where(finale, 0, base).astype(jnp.int32)


def steps_of(stream_key, dims, cuts, least, high):
    gain = 1.0
    for axis_at, blocks in cuts:
        steps = jax.random.uniform(jax.random.fold_in(jax.random.fold_in(stream_key, 6), axis_at), (blocks,), jnp.float32, least / len(cuts), high / len(cuts))
        gain = gain * jnp.repeat(jnp.exp(steps), dims[axis_at] // blocks).reshape((-1,) + (1,) * (len(dims) - 1 - axis_at))
    return gain


def centred(key, shape, scale, most, cuts=(), kind=jnp.bfloat16):
    loudness = steps_of(key, shape, cuts, -0.22, 0.18) if cuts else 1.0
    array = jax.random.normal(key, shape, jnp.float32) * scale * loudness
    return jnp.minimum(jnp.maximum(array, -most), most).astype(kind)


def setup_inputs(seed: int = 0) -> dict:
    seeds = jax.random.split(jax.random.key(seed), 6)
    return {
        "right_sides": centred(seeds[0], (BATCHES, BRHS, ROWS), 1.0, 6.0, ((2, 512),), jnp.float32),
        "inverse_diag": centred(seeds[1], (SEPS, W, W), W ** -0.5, 0.09375, ((0, 8), (1, 64)), jnp.float32),
        "lower_blocks": centred(seeds[2], (SEPS, LOWER, W), W ** -0.5, 0.09375, ((0, 8), (1, 64)), jnp.float32),
        "targets": draw_targets(jax.random.fold_in(seeds[5], 71), 0),
        "counts": draw_counts(jax.random.fold_in(seeds[5], 71), 0),
    }


def reference(right_sides, inverse_diag, lower_blocks, targets, counts):
    positions = jnp.arange(LOWER, dtype=jnp.int32) % LRD
    live = positions[None, :] < jnp.repeat(counts, LRD, axis=1)
    results = []
    for batch in range(BATCHES):
        accum = jnp.zeros((BRHS, SEPS * W), jnp.float32)
        pieces = []
        for level in range(SEPS):
            resid = right_sides[batch][:, level * W:(level + 1) * W] - accum[:, level * W:(level + 1) * W]
            solved = lax.dot_general(resid, inverse_diag[level], (((1,), (1,)), ((), ())),
                                     precision=lax.Precision.HIGHEST, preferred_element_type=jnp.float32)
            pieces.append(solved)
            update = lax.dot_general(solved, lower_blocks[level], (((1,), (1,)), ((), ())),
                                     precision=lax.Precision.HIGHEST, preferred_element_type=jnp.float32)
            update = jnp.where(live[level][None, :], update, jnp.float32(0.0))
            accum = accum.at[:, targets[level]].add(update)
        results.append(jnp.concatenate(pieces, axis=1))
    return jnp.stack(results)
```

```python
import jax
import jax.numpy as jnp
from jax import lax
from jax.sharding import PartitionSpec as P


def passed_along(block, axis, distance):
    devices = range(lax.axis_size(axis))
    route = [(i - distance, i) for i in devices if i - distance in devices]
    return lax.ppermute(block, axis, route)


def shards(right_sides, inverse_diag, lower_blocks, targets, counts):
    levels = lax.axis_size("sep")
    own_level = lax.axis_index("sep")
    batches, width_rhs, own_rows = right_sides.shape
    width = inverse_diag.shape[-1]
    given = right_sides.reshape(batches * width_rhs, own_rows)
    diag_rows = inverse_diag[0]
    lower_rows = lower_blocks[0]
    lower_count = lower_rows.shape[0]
    live = jnp.arange(lower_count, dtype=jnp.int32) < counts[0, 0]
    places = targets[0] // width * own_rows + targets[0] % own_rows

    def solve_piece(segment):
        return lax.dot_general(
            segment,
            diag_rows,
            (((1,), (1,)), ((), ())),
            precision=lax.Precision.HIGHEST,
            preferred_element_type=jnp.float32,
        )

    def lower_piece(segment):
        return lax.dot_general(
            segment,
            lower_rows,
            (((1,), (1,)), ((), ())),
            precision=lax.Precision.HIGHEST,
            preferred_element_type=jnp.float32,
        )

    def one_level(level, state):
        carried, solution = state
        resid = given - lax.dynamic_slice_in_dim(carried, level * own_rows, own_rows, 1)
        solved = solve_piece(lax.all_gather(resid, ("row", "col"), axis=1, tiled=True))
        solution = jnp.where(own_level == level, solved, solution)
        update = lower_piece(lax.all_gather(solved, ("row", "col"), axis=1, tiled=True))
        update = jnp.where(live[None, :], update, jnp.float32(0.0))
        carried = carried.at[:, places].add(update)
        return passed_along(carried, "sep", 1), solution

    carried = jnp.zeros((given.shape[0], levels * own_rows), jnp.float32)
    solution = jnp.zeros_like(given)
    carried, solution = lax.fori_loop(0, levels - 1, one_level, (carried, solution))
    last = levels - 1
    resid = given - carried[:, last * own_rows:]
    solved = solve_piece(lax.all_gather(resid, ("row", "col"), axis=1, tiled=True))
    solution = jnp.where(own_level == last, solved, solution)
    return solution.reshape(batches, width_rhs, own_rows)


def solution(mesh):
    placed = (
        P(None, None, ("sep", "row", "col")),
        P("sep", ("row", "col"), None),
        P("sep", ("row", "col"), None),
        P("sep", ("row", "col")),
        P("sep", ("row", "col")),
    )
    return jax.shard_map(
        shards,
        mesh=mesh,
        in_specs=placed,
        out_specs=P(None, None, ("sep", "row", "col")),
        check_vma=False,
    )
```

```python
import jax
import jax.numpy as jnp
from jax import lax
from jax.sharding import PartitionSpec as P


def passed_along(block, axis, distance):
    devices = range(lax.axis_size(axis))
    route = [(i - distance, i) for i in devices if i - distance in devices]
    return lax.ppermute(block, axis, route)


def gathered(block, axes):
    parts = 1
    for axis in axes:
        parts *= lax.axis_size(axis)
    copies = jnp.broadcast_to(block[None], (parts,) + block.shape)
    pieces = lax.all_to_all(copies, axes, 0, 0, tiled=True)
    return jnp.transpose(pieces, (1, 0, 2)).reshape(block.shape[0], parts * block.shape[1])


def shards(right_sides, inverse_diag, lower_blocks, targets, counts):
    levels = lax.axis_size("sep")
    own_level = lax.axis_index("sep")
    batches, width_rhs, own_rows = right_sides.shape
    width = inverse_diag.shape[-1]
    given = right_sides.reshape(batches * width_rhs, own_rows)
    diag_rows = inverse_diag[0]
    lower_rows = lower_blocks[0]
    lower_count = lower_rows.shape[0]
    live = jnp.arange(lower_count, dtype=jnp.int32) < counts[0, 0]
    places = targets[0] // width * own_rows + targets[0] % own_rows

    def solve_piece(segment):
        return lax.dot_general(
            segment,
            diag_rows,
            (((1,), (1,)), ((), ())),
            precision=lax.Precision.HIGHEST,
            preferred_element_type=jnp.float32,
        )

    def lower_piece(segment):
        return lax.dot_general(
            segment,
            lower_rows,
            (((1,), (1,)), ((), ())),
            precision=lax.Precision.HIGHEST,
            preferred_element_type=jnp.float32,
        )

    def one_level(level, state):
        carried, solution = state
        resid = given - lax.dynamic_slice_in_dim(carried, level * own_rows, own_rows, 1)
        solved = solve_piece(gathered(resid, ("row", "col")))
        solution = jnp.where(own_level == level, solved, solution)
        update = lower_piece(gathered(solved, ("row", "col")))
        update = jnp.where(live[None, :], update, jnp.float32(0.0))
        carried = carried.at[:, places].add(update)
        return passed_along(carried, "sep", 1), solution

    carried = jnp.zeros((given.shape[0], levels * own_rows), jnp.float32)
    solution = jnp.zeros_like(given)
    carried, solution = lax.fori_loop(0, levels - 1, one_level, (carried, solution))
    last = levels - 1
    resid = given - carried[:, last * own_rows:]
    solved = solve_piece(gathered(resid, ("row", "col")))
    solution = jnp.where(own_level == last, solved, solution)
    return solution.reshape(batches, width_rhs, own_rows)


def solution(mesh):
    placed = (
        P(None, None, ("sep", "row", "col")),
        P("sep", ("row", "col"), None),
        P("sep", ("row", "col"), None),
        P("sep", ("row", "col")),
        P("sep", ("row", "col")),
    )
    return jax.shard_map(
        shards,
        mesh=mesh,
        in_specs=placed,
        out_specs=P(None, None, ("sep", "row", "col")),
        check_vma=False,
    )
```

```python
import jax
import jax.numpy as jnp
from jax import lax
from jax.sharding import PartitionSpec as P


def passed_along(block, axis, distance):
    devices = range(lax.axis_size(axis))
    route = [(i - distance, i) for i in devices if i - distance in devices]
    return lax.ppermute(block, axis, route)


def stacked(block, axes):
    parts = 1
    for axis in axes:
        parts *= lax.axis_size(axis)
    flat = block.reshape(1, block.size)
    copies = jnp.broadcast_to(flat, (parts, block.size))
    pieces = lax.all_to_all(copies, axes, 0, 0, tiled=True)
    return pieces.reshape(parts * block.shape[0], block.shape[1])


def shards(right_sides, inverse_diag, lower_blocks, targets, counts):
    levels = lax.axis_size("sep")
    own_level = lax.axis_index("sep")
    batches, width_rhs, own_rows = right_sides.shape
    width = inverse_diag.shape[-1]
    axes = ("row", "col")
    given = right_sides.reshape(batches * width_rhs, own_rows).T
    diag_rows = inverse_diag[0]
    lower_rows = lower_blocks[0]
    lower_count = lower_rows.shape[0]
    live = jnp.arange(lower_count, dtype=jnp.int32) < counts[0, 0]
    places = targets[0] // width * own_rows + targets[0] % own_rows

    def times(rows, segment):
        return lax.dot_general(
            rows,
            segment,
            (((1,), (0,)), ((), ())),
            precision=lax.Precision.HIGHEST,
            preferred_element_type=jnp.float32,
        )

    def one_level(level, state):
        carried, solution = state
        resid = given - lax.dynamic_slice_in_dim(carried, level * own_rows, own_rows, 0)
        solved = times(diag_rows, stacked(resid, axes))
        solution = jnp.where(own_level == level, solved, solution)
        update = times(lower_rows, stacked(solved, axes))
        update = jnp.where(live[:, None], update, jnp.float32(0.0))
        carried = carried.at[places, :].add(update)
        return passed_along(carried, "sep", 1), solution

    carried = jnp.zeros((levels * own_rows, given.shape[1]), jnp.float32)
    solution = jnp.zeros_like(given)
    carried, solution = lax.fori_loop(0, levels - 1, one_level, (carried, solution))
    last = levels - 1
    resid = given - carried[last * own_rows:, :]
    solved = times(diag_rows, stacked(resid, axes))
    solution = jnp.where(own_level == last, solved, solution)
    return solution.T.reshape(batches, width_rhs, own_rows)


def solution(mesh):
    placed = (
        P(None, None, ("sep", "row", "col")),
        P("sep", ("row", "col"), None),
        P("sep", ("row", "col"), None),
        P("sep", ("row", "col")),
        P("sep", ("row", "col")),
    )
    return jax.shard_map(
        shards,
        mesh=mesh,
        in_specs=placed,
        out_specs=P(None, None, ("sep", "row", "col")),
        check_vma=False,
    )
```

```python
import jax
import jax.numpy as jnp
from jax import lax
from jax.sharding import PartitionSpec as P


def passed_along(block, axis, distance):
    devices = range(lax.axis_size(axis))
    route = [(i - distance, i) for i in devices if i - distance in devices]
    return lax.ppermute(block, axis, route)


def gathered(block, axes):
    parts = 1
    for axis in axes:
        parts *= lax.axis_size(axis)
    copies = jnp.broadcast_to(block.reshape(1, block.size), (parts, block.size))
    pieces = lax.all_to_all(copies, axes, 0, 0, tiled=True).reshape((parts,) + block.shape)
    return jnp.transpose(pieces, (1, 0, 2)).reshape(block.shape[0], parts * block.shape[1])


def shards(right_sides, inverse_diag, lower_blocks, targets, counts):
    levels = lax.axis_size("sep")
    own_level = lax.axis_index("sep")
    batches, width_rhs, own_rows = right_sides.shape
    width = inverse_diag.shape[-1]
    given = right_sides.reshape(batches * width_rhs, own_rows)
    diag_rows = inverse_diag[0]
    lower_rows = lower_blocks[0]
    lower_count = lower_rows.shape[0]
    live = jnp.arange(lower_count, dtype=jnp.int32) < counts[0, 0]
    places = targets[0] // width * own_rows + targets[0] % own_rows

    def solve_piece(segment):
        return lax.dot_general(
            segment,
            diag_rows,
            (((1,), (1,)), ((), ())),
            precision=lax.Precision.HIGHEST,
            preferred_element_type=jnp.float32,
        )

    def lower_piece(segment):
        return lax.dot_general(
            segment,
            lower_rows,
            (((1,), (1,)), ((), ())),
            precision=lax.Precision.HIGHEST,
            preferred_element_type=jnp.float32,
        )

    def one_level(level, state):
        carried, solution = state
        resid = given - lax.dynamic_slice_in_dim(carried, level * own_rows, own_rows, 1)
        solved = solve_piece(gathered(resid, ("row", "col")))
        solution = jnp.where(own_level == level, solved, solution)
        update = lower_piece(gathered(solved, ("row", "col")))
        update = jnp.where(live[None, :], update, jnp.float32(0.0))
        carried = carried.at[:, places].add(update)
        return passed_along(carried, "sep", 1), solution

    carried = jnp.zeros((given.shape[0], levels * own_rows), jnp.float32)
    solution = jnp.zeros_like(given)
    carried, solution = lax.fori_loop(0, levels - 1, one_level, (carried, solution))
    last = levels - 1
    resid = given - carried[:, last * own_rows:]
    solved = solve_piece(gathered(resid, ("row", "col")))
    solution = jnp.where(own_level == last, solved, solution)
    return solution.reshape(batches, width_rhs, own_rows)


def solution(mesh):
    placed = (
        P(None, None, ("sep", "row", "col")),
        P("sep", ("row", "col"), None),
        P("sep", ("row", "col"), None),
        P("sep", ("row", "col")),
        P("sep", ("row", "col")),
    )
    return jax.shard_map(
        shards,
        mesh=mesh,
        in_specs=placed,
        out_specs=P(None, None, ("sep", "row", "col")),
        check_vma=False,
    )
```

```python
import jax
import jax.numpy as jnp
from jax import lax
from jax.sharding import PartitionSpec as P


def passed_along(block, axis, distance):
    devices = range(lax.axis_size(axis))
    route = [(i - distance, i) for i in devices if i - distance in devices]
    return lax.ppermute(block, axis, route)


def gathered(block, axes):
    parts = 1
    for axis in axes:
        parts *= lax.axis_size(axis)
    copies = jnp.broadcast_to(block.reshape(1, block.size), (parts, block.size))
    pieces = lax.all_to_all(copies, axes, 0, 0, tiled=True).reshape((parts,) + block.shape)
    return jnp.transpose(pieces, (1, 0, 2)).reshape(block.shape[0], parts * block.shape[1])


def shards(right_sides, inverse_diag, lower_blocks, targets, counts):
    levels = lax.axis_size("sep")
    own_level = lax.axis_index("sep")
    batches, width_rhs, own_rows = right_sides.shape
    width = inverse_diag.shape[-1]
    given = right_sides.reshape(batches * width_rhs, own_rows)
    diag_rows = inverse_diag[0]
    lower_rows = lower_blocks[0]
    lower_count = lower_rows.shape[0]
    live = jnp.arange(lower_count, dtype=jnp.int32) < counts[0, 0]
    places = targets[0] // width * own_rows + targets[0] % own_rows
    axes = ("row", "col")

    def solve_piece(segment):
        return lax.dot_general(
            segment,
            diag_rows,
            (((1,), (1,)), ((), ())),
            precision=lax.Precision.HIGHEST,
            preferred_element_type=jnp.float32,
        )

    def lower_piece(segment):
        return lax.dot_general(
            segment,
            lower_rows,
            (((1,), (1,)), ((), ())),
            precision=lax.Precision.HIGHEST,
            preferred_element_type=jnp.float32,
        )

    own_col = lax.axis_index("col")
    group_rows = lax.all_gather(diag_rows, "col", axis=0, tiled=True)

    def finish(solved, carried):
        update = lower_piece(solved)
        update = jnp.where(live[None, :], update, jnp.float32(0.0))
        carried = carried.at[:, places].add(update)
        return passed_along(carried, "sep", 1)

    def one_level(level, state):
        carried, solution = state
        resid = given - lax.dynamic_slice_in_dim(carried, level * own_rows, own_rows, 1)
        group = lax.dot_general(
            gathered(resid, axes),
            group_rows,
            (((1,), (1,)), ((), ())),
            precision=lax.Precision.HIGHEST,
            preferred_element_type=jnp.float32,
        )
        solved = lax.dynamic_slice_in_dim(group, own_col * own_rows, own_rows, 1)
        solution = jnp.where(own_level == level, solved, solution)
        return finish(gathered(group, ("row",)), carried), solution

    solved = solve_piece(gathered(given, axes))
    solution = jnp.where(own_level == 0, solved, jnp.zeros_like(given))
    carried = jnp.zeros((given.shape[0], levels * own_rows), jnp.float32)
    carried = finish(gathered(solved, axes), carried)
    carried, solution = lax.fori_loop(1, levels - 1, one_level, (carried, solution))
    last = levels - 1
    resid = given - carried[:, last * own_rows:]
    solved = solve_piece(gathered(resid, axes))
    solution = jnp.where(own_level == last, solved, solution)
    return solution.reshape(batches, width_rhs, own_rows)


def solution(mesh):
    placed = (
        P(None, None, ("sep", "row", "col")),
        P("sep", ("row", "col"), None),
        P("sep", ("row", "col"), None),
        P("sep", ("row", "col")),
        P("sep", ("row", "col")),
    )
    return jax.shard_map(
        shards,
        mesh=mesh,
        in_specs=placed,
        out_specs=P(None, None, ("sep", "row", "col")),
        check_vma=False,
    )
```

```python
import jax
import jax.numpy as jnp
from jax import lax
from jax.sharding import PartitionSpec as P


def passed_along(block, axis, distance):
    devices = range(lax.axis_size(axis))
    route = [(i - distance, i) for i in devices if i - distance in devices]
    return lax.ppermute(block, axis, route)


def gathered(block, axes):
    parts = 1
    for axis in axes:
        parts *= lax.axis_size(axis)
    tile = (8, block.size // 8)
    copies = jnp.broadcast_to(block.reshape((1,) + tile), (parts,) + tile)
    pieces = lax.all_to_all(copies, axes, 0, 0, tiled=True).reshape((parts,) + block.shape)
    return jnp.transpose(pieces, (1, 0, 2)).reshape(block.shape[0], parts * block.shape[1])


def shards(right_sides, inverse_diag, lower_blocks, targets, counts):
    levels = lax.axis_size("sep")
    own_level = lax.axis_index("sep")
    batches, width_rhs, own_rows = right_sides.shape
    width = inverse_diag.shape[-1]
    given = right_sides.reshape(batches * width_rhs, own_rows)
    diag_rows = inverse_diag[0]
    lower_rows = lower_blocks[0]
    lower_count = lower_rows.shape[0]
    live = jnp.arange(lower_count, dtype=jnp.int32) < counts[0, 0]
    places = targets[0] // width * own_rows + targets[0] % own_rows

    def solve_piece(segment):
        return lax.dot_general(
            segment,
            diag_rows,
            (((1,), (1,)), ((), ())),
            precision=lax.Precision.HIGHEST,
            preferred_element_type=jnp.float32,
        )

    def lower_piece(segment):
        return lax.dot_general(
            segment,
            lower_rows,
            (((1,), (1,)), ((), ())),
            precision=lax.Precision.HIGHEST,
            preferred_element_type=jnp.float32,
        )

    def one_level(level, state):
        carried, solution = state
        resid = given - lax.dynamic_slice_in_dim(carried, level * own_rows, own_rows, 1)
        solved = solve_piece(gathered(resid, ("row", "col")))
        solution = jnp.where(own_level == level, solved, solution)
        update = lower_piece(gathered(solved, ("row", "col")))
        update = jnp.where(live[None, :], update, jnp.float32(0.0))
        carried = carried.at[:, places].add(update)
        return passed_along(carried, "sep", 1), solution

    carried = jnp.zeros((given.shape[0], levels * own_rows), jnp.float32)
    solution = jnp.zeros_like(given)
    carried, solution = lax.fori_loop(0, levels - 1, one_level, (carried, solution))
    last = levels - 1
    resid = given - carried[:, last * own_rows:]
    solved = solve_piece(gathered(resid, ("row", "col")))
    solution = jnp.where(own_level == last, solved, solution)
    return solution.reshape(batches, width_rhs, own_rows)


def solution(mesh):
    placed = (
        P(None, None, ("sep", "row", "col")),
        P("sep", ("row", "col"), None),
        P("sep", ("row", "col"), None),
        P("sep", ("row", "col")),
        P("sep", ("row", "col")),
    )
    return jax.shard_map(
        shards,
        mesh=mesh,
        in_specs=placed,
        out_specs=P(None, None, ("sep", "row", "col")),
        check_vma=False,
    )
```

```python
import jax
import jax.numpy as jnp
from jax import lax
from jax.sharding import PartitionSpec as P


def passed_along(block, axis, distance):
    devices = range(lax.axis_size(axis))
    route = [(i - distance, i) for i in devices if i - distance in devices]
    return lax.ppermute(block, axis, route)


def gathered(block, axes):
    parts = 1
    for axis in axes:
        parts *= lax.axis_size(axis)
    tile = (8, block.size // 8)
    copies = jnp.broadcast_to(block.reshape((1,) + tile), (parts,) + tile)
    pieces = lax.all_to_all(copies, axes, 0, 0, tiled=True).reshape((parts,) + block.shape)
    return jnp.transpose(pieces, (1, 0, 2)).reshape(block.shape[0], parts * block.shape[1])


def shards(right_sides, inverse_diag, lower_blocks, targets, counts):
    levels = lax.axis_size("sep")
    own_level = lax.axis_index("sep")
    batches, width_rhs, own_rows = right_sides.shape
    width = inverse_diag.shape[-1]
    given = right_sides.reshape(batches * width_rhs, own_rows)
    diag_rows = inverse_diag[0]
    lower_rows = lower_blocks[0]
    lower_count = lower_rows.shape[0]
    live = lax.optimization_barrier(jnp.arange(lower_count, dtype=jnp.int32)[None, :] < counts[0, 0])
    places = targets[0] // width * own_rows + targets[0] % own_rows

    def solve_piece(segment):
        return lax.dot_general(
            segment,
            diag_rows,
            (((1,), (1,)), ((), ())),
            precision=lax.Precision.HIGHEST,
            preferred_element_type=jnp.float32,
        )

    def lower_piece(segment):
        return lax.dot_general(
            segment,
            lower_rows,
            (((1,), (1,)), ((), ())),
            precision=lax.Precision.HIGHEST,
            preferred_element_type=jnp.float32,
        )

    def one_level(level, state):
        carried, solution = state
        resid = given - lax.dynamic_slice_in_dim(carried, level * own_rows, own_rows, 1)
        solved = solve_piece(gathered(resid, ("row", "col")))
        solution = jnp.where(own_level == level, solved, solution)
        update = lower_piece(gathered(solved, ("row", "col")))
        update = jnp.where(live, update, jnp.float32(0.0))
        carried = carried.at[:, places].add(update)
        return passed_along(carried, "sep", 1), solution

    carried = jnp.zeros((given.shape[0], levels * own_rows), jnp.float32)
    solution = jnp.zeros_like(given)
    carried, solution = lax.fori_loop(0, levels - 1, one_level, (carried, solution))
    last = levels - 1
    resid = given - carried[:, last * own_rows:]
    solved = solve_piece(gathered(resid, ("row", "col")))
    solution = jnp.where(own_level == last, solved, solution)
    return solution.reshape(batches, width_rhs, own_rows)


def solution(mesh):
    placed = (
        P(None, None, ("sep", "row", "col")),
        P("sep", ("row", "col"), None),
        P("sep", ("row", "col"), None),
        P("sep", ("row", "col")),
        P("sep", ("row", "col")),
    )
    return jax.shard_map(
        shards,
        mesh=mesh,
        in_specs=placed,
        out_specs=P(None, None, ("sep", "row", "col")),
        check_vma=False,
    )
```
